512 devices in a mesh: atom: 4 (over x), tm: 4 (over y_hi), wave: 32 (over y_lo, z, core).
Axes of the slice: x: 4, y: 8 (y_hi: 4, y_lo: 2; y = y_hi * 2 + y_lo), z: 8, core: 2. Of those that a mesh axis runs over, the one named last changes fastest.
Arguments:
- positions: float32 [64, 3, 8192], P('tm', None, ('atom', 'wave')), may hold values from 0 to 1
- species: int32 [8192], P('atom'), may hold values 0 or 1
- kx_index: int32 [16], replicated, may hold values from 1 to 16
- kyz_index: int32 [2, 4096], P(None, 'wave'), may hold values from -16 to 16
Outputs:
- spectra: float32 [3, 64, 16, 4096], P(None, None, ('atom', 'tm'), 'wave')
- densities: float32 [64, 2, 2, 16, 4096], P('tm', None, None, 'atom', 'wave')
The draws below stay inside these ranges and needn't reach their ends.
Inputs may be any that keep to these rules, and one draw needn't show every extreme that they name: `species`: 0 marks an oxygen atom, 1 a hydrogen atom.
All inputs are finite; a program needn't handle non-finite values. No bound on the sum of `species` on one device may be relied on, other than what follows from the above.
Results may differ from the reference program's by a relative error of at most 0.0034.
Values sent between devices are 32-bit elements; how exact they have to be, the bound alone decides.
No kernel may reach another device: no remote copies, remote signals or barrier semaphores. Data moves between devices by JAX's collectives and lax.ppermute only.
A program may use at most 64 MiB of HBM per device.

```python
import math
import jax
import jax.numpy as jnp
from jax import lax

FRAMES = 64
KX = 16
N_ATOMS = 8192
KYZ = 4096


def set_ends(entries, own_key, smallest, largest):
    dims = entries.shape
    index_at = [jax.random.randint(jax.random.fold_in(own_key, axis), (), 0, dims[axis]) for axis in range(len(dims))]
    entries = entries.at[tuple(index_at)].set(smallest)
    longest = dims.index(max(dims))
    index_at[longest] = (index_at[longest] + 1) % dims[longest]
    return entries.at[tuple(index_at)].set(largest)


def levels(rng, shape, split, least, largest):
    def one(position, parts):
        draws = jax.random.uniform(jax.random.fold_in(jax.random.fold_in(rng, 6), position), (parts,), jnp.float32, least / len(split), largest / len(split))
        return jnp.repeat(jnp.exp(draws), shape[position] // parts).reshape((-1,) + (1,) * (len(shape) - position - 1))

    factor_of = one(*split[0])
    for cut in split[1:]:
        factor_of = factor_of * one(*cut)
    return factor_of


def setup_inputs(seed: int = 0) -> dict:
    seeds = jax.random.split(jax.random.key(seed), 5)
    return {
        "positions": jnp.clip(1.0 * jax.random.uniform(seeds[0], (FRAMES, 3, N_ATOMS), jnp.float32) ** levels(seeds[0], (FRAMES, 3, N_ATOMS), ((0, 4), (2, 128)), -0.2, 0.2), 0.0, 1.0),
        "species": set_ends((jax.random.randint(seeds[1], (N_ATOMS,), 0, 3) < 2).astype(jnp.int32), jax.random.fold_in(seeds[1], 1), 0, 1),
        "kx_index": set_ends(jax.random.randint(seeds[2], (KX,), 1, 17), jax.random.fold_in(seeds[2], 1), 1, 16).astype(jnp.int32),
        "kyz_index": set_ends(jax.random.randint(seeds[3], (2, KYZ), -16, 17), jax.random.fold_in(seeds[3], 1), -16, 16).astype(jnp.int32),
    }


TWO_PI = 2.0 * math.pi

def frac_turns(values):
    return values - jnp.floor(values)

def hann_window(length):
    frame_steps = jnp.arange(length).astype(jnp.float32)
    return 0.5 - 0.5 * jnp.cos(TWO_PI / length * (frame_steps + 0.5))

def combine(products):
    real_part = products[:, 0, :, 0] - products[:, 1, :, 1]
    imag_part = -(products[:, 1, :, 0] + products[:, 0, :, 1])
    return jnp.stack([real_part, imag_part], axis=1)

def axis_tables(coord):
    index_values = (jnp.arange(33) - 16).astype(jnp.float32)
    angle = TWO_PI * frac_turns(coord[:, None] * index_values[None, :])
    return (jnp.cos(angle), jnp.sin(angle))

def reference(positions, species, kx_index, kyz_index):
    atom_total = positions.shape[2]
    block_width = min(KYZ, 512)
    blocks = KYZ // block_width
    onehot = jnp.stack([species == 0, species == 1]).astype(jnp.float32)
    kx_real = kx_index.astype(jnp.float32)
    ky_blocks = (kyz_index[0] + 16).astype(jnp.int32).reshape(blocks, block_width)
    kz_blocks = (kyz_index[1] + 16).astype(jnp.int32).reshape(blocks, block_width)

    def one_frame(coords):
        x_angle = TWO_PI * frac_turns(kx_real[:, None] * coords[0][None, :])
        phases = jnp.stack([jnp.cos(x_angle), jnp.sin(x_angle)])
        x_table = (onehot[:, None, None, :] * phases[None]).astype(jnp.bfloat16)
        x_table = lax.optimization_barrier(x_table).astype(jnp.float32).reshape(4 * KX, atom_total)
        cos_y, sin_y = axis_tables(coords[1])
        cos_z, sin_z = axis_tables(coords[2])

        def one_block(wave_pair):
            ky_block, kz_block = wave_pair
            cy = jnp.take(cos_y, ky_block, axis=1)
            sy = jnp.take(sin_y, ky_block, axis=1)
            cz = jnp.take(cos_z, kz_block, axis=1)
            sz = jnp.take(sin_z, kz_block, axis=1)
            yz_cos = cy * cz - sy * sz
            yz_sin = sy * cz + cy * sz
            yz_table = jnp.concatenate([yz_cos, yz_sin], axis=1).astype(jnp.bfloat16)
            yz_table = lax.optimization_barrier(yz_table).astype(jnp.float32)
            products = jnp.dot(x_table, yz_table, precision=lax.Precision.HIGHEST)
            return combine(products.reshape(2, 2, KX, 2, block_width))
        block_parts = lax.map(one_block, (ky_blocks, kz_blocks))
        return jnp.transpose(block_parts, (1, 2, 3, 0, 4)).reshape(2, 2, KX, KYZ)
    densities = lax.map(one_frame, positions) / jnp.sqrt(jnp.float32(atom_total))
    window = hann_window(FRAMES)
    energy = jnp.sum(window * window)
    complex_series = (densities[:, :, 0] + 1j * densities[:, :, 1]) * window[:, None, None, None]
    transformed = jnp.fft.fft(complex_series, axis=0)
    first = transformed[:, 0]
    second = transformed[:, 1]
    spectra = jnp.stack([jnp.real(first * jnp.conj(first)), jnp.real(first * jnp.conj(second)), jnp.real(second * jnp.conj(second))]) / energy
    return (spectra, densities)
```

```python
import math

import jax
import jax.numpy as jnp
from jax import lax
from jax.experimental import pallas as pl
from jax.experimental.pallas import tpu as pltpu
from jax.sharding import PartitionSpec as P

TWO_PI = 2.0 * math.pi


def copy_for_each(shard, axis):
    peers = lax.axis_size(axis)
    return lax.all_to_all(
        jnp.broadcast_to(shard[None], (peers, *shard.shape)), axis, 0, 0, tiled=True
    )


def joined_along(pieces, dim):
    pieces = jnp.moveaxis(pieces, 0, dim)
    dims = pieces.shape
    return pieces.reshape(*dims[:dim], dims[dim] * dims[dim + 1], *dims[dim + 2 :])


def gathered_copies(shard, axis, dim):
    pieces = copy_for_each(shard, axis)
    return joined_along(pieces, dim)


def cut_along(shard, dim, peers):
    dims = shard.shape
    pieces = shard.reshape(*dims[:dim], peers, dims[dim] // peers, *dims[dim + 1 :])
    return jnp.moveaxis(pieces, dim, 0)


def sent_and_summed(shard, axis, dim):
    pieces = cut_along(shard, dim, lax.axis_size(axis))
    arrived = lax.all_to_all(pieces, axis, split_axis=0, concat_axis=0, tiled=True)
    return arrived.sum(axis=0)


def frac_turns(values):
    return values - jnp.floor(values)


def hann_window(length):
    frame_steps = jnp.arange(length).astype(jnp.float32)
    return 0.5 - 0.5 * jnp.cos(TWO_PI / length * (frame_steps + 0.5))


def combine(products):
    real_part = products[:, 0, :, 0] - products[:, 1, :, 1]
    imag_part = -(products[:, 1, :, 0] + products[:, 0, :, 1])
    return jnp.stack([real_part, imag_part], axis=1)


def transform(series):
    length = series.shape[0]
    window = hann_window(length)
    energy = jnp.sum(window * window)
    weighted = series * window[:, None, None, None, None]
    frame_steps = jnp.arange(length)
    phase_turns = (frame_steps[:, None] * frame_steps[None, :] % length).astype(jnp.float32)
    dft_angle = TWO_PI / length * phase_turns
    cos_table = jnp.cos(dft_angle)
    sin_table = jnp.sin(dft_angle)
    real_part = weighted[:, :, 0]
    imag_part = weighted[:, :, 1]
    highest = lax.Precision.HIGHEST
    spec_real = jnp.einsum("ft,tsmj->fsmj", cos_table, real_part, precision=highest) + jnp.einsum(
        "ft,tsmj->fsmj", sin_table, imag_part, precision=highest
    )
    spec_imag = jnp.einsum("ft,tsmj->fsmj", cos_table, imag_part, precision=highest) - jnp.einsum(
        "ft,tsmj->fsmj", sin_table, real_part, precision=highest
    )
    oxygen_pair = spec_real[:, 0] * spec_real[:, 0] + spec_imag[:, 0] * spec_imag[:, 0]
    cross_pair = spec_real[:, 0] * spec_real[:, 1] + spec_imag[:, 0] * spec_imag[:, 1]
    hydrogen_pair = spec_real[:, 1] * spec_real[:, 1] + spec_imag[:, 1] * spec_imag[:, 1]
    return jnp.stack([oxygen_pair, cross_pair, hydrogen_pair]) / energy


def power_rows(base_cos, base_sin, count):
    rows = [(jnp.ones_like(base_cos), jnp.zeros_like(base_sin)), (base_cos, base_sin)]
    for _ in range(count - 1):
        prev_cos, prev_sin = rows[-1]
        rows.append((prev_cos * base_cos - prev_sin * base_sin, prev_sin * base_cos + prev_cos * base_sin))
    return rows


def split_dot(picks, table):
    high = table.astype(jnp.bfloat16)
    low = (table - high.astype(jnp.float32)).astype(jnp.bfloat16)
    dims = (((1,), (0,)), ((), ()))
    return lax.dot_general(picks, high, dims, preferred_element_type=jnp.float32) + lax.dot_general(
        picks, low, dims, preferred_element_type=jnp.float32
    )


def frame_kernel(base_ref, onehot_ref, pick_x_ref, pick_y_ref, pick_z_ref, out_ref, axis_ref, x_ref):
    base = base_ref[0]
    kmax = 16
    rows_pad = axis_ref.shape[1]
    for axis in range(2):
        powers = power_rows(base[2 + 2 * axis : 3 + 2 * axis], base[3 + 2 * axis : 4 + 2 * axis], kmax)
        for k, (cos_k, sin_k) in enumerate(powers):
            axis_ref[2 * axis, kmax + k : kmax + k + 1, :] = cos_k
            axis_ref[2 * axis + 1, kmax + k : kmax + k + 1, :] = sin_k
            if k:
                axis_ref[2 * axis, kmax - k : kmax - k + 1, :] = cos_k
                axis_ref[2 * axis + 1, kmax - k : kmax - k + 1, :] = -sin_k
        pad = rows_pad - (2 * kmax + 1)
        zeros = jnp.zeros((pad, base.shape[1]), jnp.float32)
        axis_ref[2 * axis, 2 * kmax + 1 :, :] = zeros
        axis_ref[2 * axis + 1, 2 * kmax + 1 :, :] = zeros
    x_powers = power_rows(base[0:1], base[1:2], kmax)
    for k in range(1, kmax + 1):
        x_ref[0, k - 1 : k, :] = x_powers[k][0]
        x_ref[1, k - 1 : k, :] = x_powers[k][1]
    pick_x = pick_x_ref[...]
    pick_y = pick_y_ref[...]
    pick_z = pick_z_ref[...]
    cy = split_dot(pick_y, axis_ref[0])
    sy = split_dot(pick_y, axis_ref[1])
    cz = split_dot(pick_z, axis_ref[2])
    sz = split_dot(pick_z, axis_ref[3])
    yz_cos = (cy * cz - sy * sz).astype(jnp.bfloat16)
    yz_sin = (sy * cz + cy * sz).astype(jnp.bfloat16)
    x_cos = split_dot(pick_x, x_ref[0])
    x_sin = split_dot(pick_x, x_ref[1])
    onehot = onehot_ref[...]
    x_table = jnp.concatenate(
        [onehot[0:1] * x_cos, onehot[0:1] * x_sin, onehot[1:2] * x_cos, onehot[1:2] * x_sin], axis=0
    ).astype(jnp.bfloat16)
    dims = (((1,), (1,)), ((), ()))
    with_cos = lax.dot_general(x_table, yz_cos, dims, preferred_element_type=jnp.float32)
    with_sin = lax.dot_general(x_table, yz_sin, dims, preferred_element_type=jnp.float32)
    kx = kmax
    for s in range(2):
        cos_rows = slice((2 * s) * kx, (2 * s + 1) * kx)
        sin_rows = slice((2 * s + 1) * kx, (2 * s + 2) * kx)
        out_ref[0, s, 0] = with_cos[cos_rows] - with_sin[sin_rows]
        out_ref[0, s, 1] = -(with_sin[cos_rows] + with_cos[sin_rows])


def picks_of(index, lowest, count):
    cols = jnp.arange(count, dtype=jnp.int32)
    return (index[:, None] - lowest == cols[None, :]).astype(jnp.bfloat16)


def local(positions, species, kx_index, kyz_index):
    local_frames = positions.shape[0]
    kx_count = kx_index.shape[0]
    kyz_local = kyz_index.shape[1]
    total_atoms = positions.shape[2] * lax.axis_size("atom") * lax.axis_size("wave")
    onehot_all = jnp.stack([species == 0, species == 1]).astype(jnp.float32)
    block_coords = gathered_copies(positions, "wave", 2)
    atom_count = block_coords.shape[2]
    angle = TWO_PI * frac_turns(block_coords)
    base = jnp.stack([jnp.cos(angle), jnp.sin(angle)], axis=2).reshape(local_frames, 6, atom_count)
    rows_pad = 48
    pick_x = picks_of(kx_index, 1, 16)
    pick_y = picks_of(kyz_index[0], -16, rows_pad)
    pick_z = picks_of(kyz_index[1], -16, rows_pad)
    partial_value = pl.pallas_call(
        frame_kernel,
        grid=(local_frames,),
        in_specs=[
            pl.BlockSpec((1, 6, atom_count), lambda t: (t, 0, 0)),
            pl.BlockSpec((2, atom_count), lambda t: (0, 0)),
            pl.BlockSpec((kx_count, 16), lambda t: (0, 0)),
            pl.BlockSpec((kyz_local, rows_pad), lambda t: (0, 0)),
            pl.BlockSpec((kyz_local, rows_pad), lambda t: (0, 0)),
        ],
        out_specs=pl.BlockSpec((1, 2, 2, kx_count, kyz_local), lambda t: (t, 0, 0, 0, 0)),
        out_shape=jax.ShapeDtypeStruct((local_frames, 2, 2, kx_count, kyz_local), jnp.float32),
        scratch_shapes=[
            pltpu.VMEM((4, rows_pad, atom_count), jnp.float32),
            pltpu.VMEM((2, 16, atom_count), jnp.float32),
        ],
    )(base, onehot_all, pick_x, pick_y, pick_z)
    owned = sent_and_summed(partial_value, "atom", 3)
    densities = owned / jnp.sqrt(jnp.float32(total_atoms))
    spectra = transform(lax.all_to_all(densities, "tm", split_axis=3, concat_axis=0, tiled=True))
    return (spectra, densities)


def solution(mesh):
    in_specs = (P("tm", None, ("atom", "wave")), P("atom"), P(), P(None, "wave"))
    out_specs = (P(None, None, ("atom", "tm"), "wave"), P("tm", None, None, "atom", "wave"))
    return jax.shard_map(local, mesh=mesh, in_specs=in_specs, out_specs=out_specs, check_vma=False)
```

```python
import math

import jax
import jax.numpy as jnp
from jax import lax
from jax.experimental import pallas as pl
from jax.experimental.pallas import tpu as pltpu
from jax.sharding import PartitionSpec as P

TWO_PI = 2.0 * math.pi


def copy_for_each(shard, axis):
    peers = lax.axis_size(axis)
    return lax.all_to_all(
        jnp.broadcast_to(shard[None], (peers, *shard.shape)), axis, 0, 0, tiled=True
    )


def joined_along(pieces, dim):
    pieces = jnp.moveaxis(pieces, 0, dim)
    dims = pieces.shape
    return pieces.reshape(*dims[:dim], dims[dim] * dims[dim + 1], *dims[dim + 2 :])


def gathered_copies(shard, axis, dim):
    pieces = copy_for_each(shard, axis)
    return joined_along(pieces, dim)


def cut_along(shard, dim, peers):
    dims = shard.shape
    pieces = shard.reshape(*dims[:dim], peers, dims[dim] // peers, *dims[dim + 1 :])
    return jnp.moveaxis(pieces, dim, 0)


def sent_and_summed(shard, axis, dim):
    pieces = cut_along(shard, dim, lax.axis_size(axis))
    arrived = lax.all_to_all(pieces, axis, split_axis=0, concat_axis=0, tiled=True)
    return arrived.sum(axis=0)


def frac_turns(values):
    return values - jnp.floor(values)


def hann_window(length):
    frame_steps = jnp.arange(length).astype(jnp.float32)
    return 0.5 - 0.5 * jnp.cos(TWO_PI / length * (frame_steps + 0.5))


def combine(products):
    real_part = products[:, 0, :, 0] - products[:, 1, :, 1]
    imag_part = -(products[:, 1, :, 0] + products[:, 0, :, 1])
    return jnp.stack([real_part, imag_part], axis=1)


def transform(series):
    length = series.shape[0]
    window = hann_window(length)
    energy = jnp.sum(window * window)
    weighted = series * window[:, None, None, None, None]
    frame_steps = jnp.arange(length)
    phase_turns = (frame_steps[:, None] * frame_steps[None, :] % length).astype(jnp.float32)
    dft_angle = TWO_PI / length * phase_turns
    cos_table = jnp.cos(dft_angle)
    sin_table = jnp.sin(dft_angle)
    real_part = weighted[:, :, 0]
    imag_part = weighted[:, :, 1]
    highest = lax.Precision.HIGHEST
    spec_real = jnp.einsum("ft,tsmj->fsmj", cos_table, real_part, precision=highest) + jnp.einsum(
        "ft,tsmj->fsmj", sin_table, imag_part, precision=highest
    )
    spec_imag = jnp.einsum("ft,tsmj->fsmj", cos_table, imag_part, precision=highest) - jnp.einsum(
        "ft,tsmj->fsmj", sin_table, real_part, precision=highest
    )
    oxygen_pair = spec_real[:, 0] * spec_real[:, 0] + spec_imag[:, 0] * spec_imag[:, 0]
    cross_pair = spec_real[:, 0] * spec_real[:, 1] + spec_imag[:, 0] * spec_imag[:, 1]
    hydrogen_pair = spec_real[:, 1] * spec_real[:, 1] + spec_imag[:, 1] * spec_imag[:, 1]
    return jnp.stack([oxygen_pair, cross_pair, hydrogen_pair]) / energy


def power_rows(base_cos, base_sin, count):
    rows = [(jnp.ones_like(base_cos), jnp.zeros_like(base_sin)), (base_cos, base_sin)]
    for _ in range(count - 1):
        prev_cos, prev_sin = rows[-1]
        rows.append((prev_cos * base_cos - prev_sin * base_sin, prev_sin * base_cos + prev_cos * base_sin))
    return rows


def split_dot(picks, table, stacked):
    rows = table.shape[0]
    high = table.astype(jnp.bfloat16)
    stacked[0:rows, :] = high
    stacked[rows : 2 * rows, :] = (table - high.astype(jnp.float32)).astype(jnp.bfloat16)
    dims = (((1,), (0,)), ((), ()))
    return lax.dot_general(picks, stacked[...], dims, preferred_element_type=jnp.float32)


def frame_kernel(base_ref, onehot_ref, pick_x_ref, pick_y_ref, pick_z_ref, out_ref, axis_ref, x_ref, yz_half, x_half):
    base = base_ref[0]
    kmax = 16
    rows_pad = axis_ref.shape[1]
    for axis in range(2):
        powers = power_rows(base[2 + 2 * axis : 3 + 2 * axis], base[3 + 2 * axis : 4 + 2 * axis], kmax)
        for k, (cos_k, sin_k) in enumerate(powers):
            axis_ref[2 * axis, kmax + k : kmax + k + 1, :] = cos_k
            axis_ref[2 * axis + 1, kmax + k : kmax + k + 1, :] = sin_k
            if k:
                axis_ref[2 * axis, kmax - k : kmax - k + 1, :] = cos_k
                axis_ref[2 * axis + 1, kmax - k : kmax - k + 1, :] = -sin_k
        pad = rows_pad - (2 * kmax + 1)
        zeros = jnp.zeros((pad, base.shape[1]), jnp.float32)
        axis_ref[2 * axis, 2 * kmax + 1 :, :] = zeros
        axis_ref[2 * axis + 1, 2 * kmax + 1 :, :] = zeros
    x_powers = power_rows(base[0:1], base[1:2], kmax)
    for k in range(1, kmax + 1):
        x_ref[0, k - 1 : k, :] = x_powers[k][0]
        x_ref[1, k - 1 : k, :] = x_powers[k][1]
    pick_x = pick_x_ref[...]
    pick_y = pick_y_ref[...]
    pick_z = pick_z_ref[...]
    cy = split_dot(pick_y, axis_ref[0], yz_half.at[0])
    sy = split_dot(pick_y, axis_ref[1], yz_half.at[1])
    cz = split_dot(pick_z, axis_ref[2], yz_half.at[2])
    sz = split_dot(pick_z, axis_ref[3], yz_half.at[3])
    yz_cos = (cy * cz - sy * sz).astype(jnp.bfloat16)
    yz_sin = (sy * cz + cy * sz).astype(jnp.bfloat16)
    x_cos = split_dot(pick_x, x_ref[0], x_half.at[0])
    x_sin = split_dot(pick_x, x_ref[1], x_half.at[1])
    onehot = onehot_ref[...]
    x_table = jnp.concatenate(
        [onehot[0:1] * x_cos, onehot[0:1] * x_sin, onehot[1:2] * x_cos, onehot[1:2] * x_sin], axis=0
    ).astype(jnp.bfloat16)
    dims = (((1,), (1,)), ((), ()))
    with_cos = lax.dot_general(x_table, yz_cos, dims, preferred_element_type=jnp.float32)
    with_sin = lax.dot_general(x_table, yz_sin, dims, preferred_element_type=jnp.float32)
    kx = kmax
    for s in range(2):
        cos_rows = slice((2 * s) * kx, (2 * s + 1) * kx)
        sin_rows = slice((2 * s + 1) * kx, (2 * s + 2) * kx)
        out_ref[0, s, 0] = with_cos[cos_rows] - with_sin[sin_rows]
        out_ref[0, s, 1] = -(with_sin[cos_rows] + with_cos[sin_rows])


def picks_of(index, lowest, count):
    cols = jnp.arange(count, dtype=jnp.int32)
    picks = (index[:, None] - lowest == cols[None, :]).astype(jnp.bfloat16)
    return jnp.concatenate([picks, picks], axis=1)


def local(positions, species, kx_index, kyz_index):
    local_frames = positions.shape[0]
    kx_count = kx_index.shape[0]
    kyz_local = kyz_index.shape[1]
    total_atoms = positions.shape[2] * lax.axis_size("atom") * lax.axis_size("wave")
    onehot_all = jnp.stack([species == 0, species == 1]).astype(jnp.float32)
    block_coords = lax.all_gather(positions, "wave", axis=2, tiled=True)
    atom_count = block_coords.shape[2]
    angle = TWO_PI * frac_turns(block_coords)
    base = jnp.stack([jnp.cos(angle), jnp.sin(angle)], axis=2).reshape(local_frames, 6, atom_count)
    rows_pad = 48
    pick_x = picks_of(kx_index, 1, 16)
    pick_y = picks_of(kyz_index[0], -16, rows_pad)
    pick_z = picks_of(kyz_index[1], -16, rows_pad)
    partial_value = pl.pallas_call(
        frame_kernel,
        grid=(local_frames,),
        in_specs=[
            pl.BlockSpec((1, 6, atom_count), lambda t: (t, 0, 0)),
            pl.BlockSpec((2, atom_count), lambda t: (0, 0)),
            pl.BlockSpec((kx_count, 32), lambda t: (0, 0)),
            pl.BlockSpec((kyz_local, 2 * rows_pad), lambda t: (0, 0)),
            pl.BlockSpec((kyz_local, 2 * rows_pad), lambda t: (0, 0)),
        ],
        out_specs=pl.BlockSpec((1, 2, 2, kx_count, kyz_local), lambda t: (t, 0, 0, 0, 0)),
        out_shape=jax.ShapeDtypeStruct((local_frames, 2, 2, kx_count, kyz_local), jnp.float32),
        scratch_shapes=[
            pltpu.VMEM((4, rows_pad, atom_count), jnp.float32),
            pltpu.VMEM((2, 16, atom_count), jnp.float32),
            pltpu.VMEM((4, 2 * rows_pad, atom_count), jnp.bfloat16),
            pltpu.VMEM((2, 32, atom_count), jnp.bfloat16),
        ],
    )(base, onehot_all, pick_x, pick_y, pick_z)
    owned = lax.psum_scatter(partial_value, "atom", scatter_dimension=3, tiled=True)
    densities = owned / jnp.sqrt(jnp.float32(total_atoms))
    spectra = transform(lax.all_to_all(densities, "tm", split_axis=3, concat_axis=0, tiled=True))
    return (spectra, densities)


def solution(mesh):
    in_specs = (P("tm", None, ("atom", "wave")), P("atom"), P(), P(None, "wave"))
    out_specs = (P(None, None, ("atom", "tm"), "wave"), P("tm", None, None, "atom", "wave"))
    return jax.shard_map(local, mesh=mesh, in_specs=in_specs, out_specs=out_specs, check_vma=False)
```

```python
import math

import jax
import jax.numpy as jnp
from jax import lax
from jax.experimental import pallas as pl
from jax.experimental.pallas import tpu as pltpu
from jax.sharding import PartitionSpec as P

TWO_PI = 2.0 * math.pi


def copy_for_each(shard, axis):
    peers = lax.axis_size(axis)
    return lax.all_to_all(
        jnp.broadcast_to(shard[None], (peers, *shard.shape)), axis, 0, 0, tiled=True
    )


def joined_along(pieces, dim):
    pieces = jnp.moveaxis(pieces, 0, dim)
    dims = pieces.shape
    return pieces.reshape(*dims[:dim], dims[dim] * dims[dim + 1], *dims[dim + 2 :])


def gathered_copies(shard, axis, dim):
    pieces = copy_for_each(shard, axis)
    return joined_along(pieces, dim)


def cut_along(shard, dim, peers):
    dims = shard.shape
    pieces = shard.reshape(*dims[:dim], peers, dims[dim] // peers, *dims[dim + 1 :])
    return jnp.moveaxis(pieces, dim, 0)


def sent_and_summed(shard, axis, dim):
    pieces = cut_along(shard, dim, lax.axis_size(axis))
    arrived = lax.all_to_all(pieces, axis, split_axis=0, concat_axis=0, tiled=True)
    return arrived.sum(axis=0)


def frac_turns(values):
    return values - jnp.floor(values)


def hann_window(length):
    frame_steps = jnp.arange(length).astype(jnp.float32)
    return 0.5 - 0.5 * jnp.cos(TWO_PI / length * (frame_steps + 0.5))


def combine(products):
    real_part = products[:, 0, :, 0] - products[:, 1, :, 1]
    imag_part = -(products[:, 1, :, 0] + products[:, 0, :, 1])
    return jnp.stack([real_part, imag_part], axis=1)


def transform(series):
    length = series.shape[0]
    window = hann_window(length)
    energy = jnp.sum(window * window)
    weighted = series * window[:, None, None, None, None]
    frame_steps = jnp.arange(length)
    phase_turns = (frame_steps[:, None] * frame_steps[None, :] % length).astype(jnp.float32)
    dft_angle = TWO_PI / length * phase_turns
    cos_table = jnp.cos(dft_angle)
    sin_table = jnp.sin(dft_angle)
    real_part = weighted[:, :, 0]
    imag_part = weighted[:, :, 1]
    highest = lax.Precision.HIGHEST
    spec_real = jnp.einsum("ft,tsmj->fsmj", cos_table, real_part, precision=highest) + jnp.einsum(
        "ft,tsmj->fsmj", sin_table, imag_part, precision=highest
    )
    spec_imag = jnp.einsum("ft,tsmj->fsmj", cos_table, imag_part, precision=highest) - jnp.einsum(
        "ft,tsmj->fsmj", sin_table, real_part, precision=highest
    )
    oxygen_pair = spec_real[:, 0] * spec_real[:, 0] + spec_imag[:, 0] * spec_imag[:, 0]
    cross_pair = spec_real[:, 0] * spec_real[:, 1] + spec_imag[:, 0] * spec_imag[:, 1]
    hydrogen_pair = spec_real[:, 1] * spec_real[:, 1] + spec_imag[:, 1] * spec_imag[:, 1]
    return jnp.stack([oxygen_pair, cross_pair, hydrogen_pair]) / energy


def power_rows(base_cos, base_sin, count):
    rows = [(jnp.ones_like(base_cos), jnp.zeros_like(base_sin)), (base_cos, base_sin)]
    for _ in range(count - 1):
        prev_cos, prev_sin = rows[-1]
        rows.append((prev_cos * base_cos - prev_sin * base_sin, prev_sin * base_cos + prev_cos * base_sin))
    return rows


def split_dot(picks, table, stacked):
    rows = table.shape[0]
    high = table.astype(jnp.bfloat16)
    stacked[0:rows, :] = high
    stacked[rows : 2 * rows, :] = (table - high.astype(jnp.float32)).astype(jnp.bfloat16)
    dims = (((1,), (0,)), ((), ()))
    return lax.dot_general(picks, stacked[...], dims, preferred_element_type=jnp.float32)


def frame_kernel(base_ref, onehot_ref, pick_x_ref, pick_y_ref, pick_z_ref, out_ref, axis_ref, x_ref, yz_half, x_half):
    base = base_ref[0]
    kmax = 16
    rows_pad = axis_ref.shape[1]
    for axis in range(2):
        powers = power_rows(base[2 + 2 * axis : 3 + 2 * axis], base[3 + 2 * axis : 4 + 2 * axis], kmax)
        for k, (cos_k, sin_k) in enumerate(powers):
            axis_ref[2 * axis, kmax + k : kmax + k + 1, :] = cos_k
            axis_ref[2 * axis + 1, kmax + k : kmax + k + 1, :] = sin_k
            if k:
                axis_ref[2 * axis, kmax - k : kmax - k + 1, :] = cos_k
                axis_ref[2 * axis + 1, kmax - k : kmax - k + 1, :] = -sin_k
        pad = rows_pad - (2 * kmax + 1)
        zeros = jnp.zeros((pad, base.shape[1]), jnp.float32)
        axis_ref[2 * axis, 2 * kmax + 1 :, :] = zeros
        axis_ref[2 * axis + 1, 2 * kmax + 1 :, :] = zeros
    x_powers = power_rows(base[0:1], base[1:2], kmax)
    for k in range(1, kmax + 1):
        x_ref[0, k - 1 : k, :] = x_powers[k][0]
        x_ref[1, k - 1 : k, :] = x_powers[k][1]
    pick_x = pick_x_ref[...]
    pick_y = pick_y_ref[...]
    pick_z = pick_z_ref[...]
    cy = split_dot(pick_y, axis_ref[0], yz_half.at[0])
    sy = split_dot(pick_y, axis_ref[1], yz_half.at[1])
    cz = split_dot(pick_z, axis_ref[2], yz_half.at[2])
    sz = split_dot(pick_z, axis_ref[3], yz_half.at[3])
    yz_cos = (cy * cz - sy * sz).astype(jnp.bfloat16)
    yz_sin = (sy * cz + cy * sz).astype(jnp.bfloat16)
    x_cos = split_dot(pick_x, x_ref[0], x_half.at[0])
    x_sin = split_dot(pick_x, x_ref[1], x_half.at[1])
    onehot = onehot_ref[...]
    x_table = jnp.concatenate(
        [onehot[0:1] * x_cos, onehot[0:1] * x_sin, onehot[1:2] * x_cos, onehot[1:2] * x_sin], axis=0
    ).astype(jnp.bfloat16)
    dims = (((1,), (1,)), ((), ()))
    with_cos = lax.dot_general(x_table, yz_cos, dims, preferred_element_type=jnp.float32)
    with_sin = lax.dot_general(x_table, yz_sin, dims, preferred_element_type=jnp.float32)
    kx = kmax
    for s in range(2):
        cos_rows = slice((2 * s) * kx, (2 * s + 1) * kx)
        sin_rows = slice((2 * s + 1) * kx, (2 * s + 2) * kx)
        out_ref[0, s, 0] = with_cos[cos_rows] - with_sin[sin_rows]
        out_ref[0, s, 1] = -(with_sin[cos_rows] + with_cos[sin_rows])


def picks_of(index, lowest, count):
    cols = jnp.arange(count, dtype=jnp.int32)
    picks = (index[:, None] - lowest == cols[None, :]).astype(jnp.bfloat16)
    return jnp.concatenate([picks, picks], axis=1)


def local(positions, species, kx_index, kyz_index):
    local_frames = positions.shape[0]
    kx_count = kx_index.shape[0]
    kyz_local = kyz_index.shape[1]
    total_atoms = positions.shape[2] * lax.axis_size("atom") * lax.axis_size("wave")
    onehot_all = jnp.stack([species == 0, species == 1]).astype(jnp.float32)
    block_coords = gathered_copies(positions, "wave", 2)
    atom_count = block_coords.shape[2]
    angle = TWO_PI * frac_turns(block_coords)
    base = jnp.stack([jnp.cos(angle), jnp.sin(angle)], axis=2).reshape(local_frames, 6, atom_count)
    rows_pad = 48
    pick_x = picks_of(kx_index, 1, 16)
    pick_y = picks_of(kyz_index[0], -16, rows_pad)
    pick_z = picks_of(kyz_index[1], -16, rows_pad)
    partial_value = pl.pallas_call(
        frame_kernel,
        grid=(local_frames,),
        in_specs=[
            pl.BlockSpec((1, 6, atom_count), lambda t: (t, 0, 0)),
            pl.BlockSpec((2, atom_count), lambda t: (0, 0)),
            pl.BlockSpec((kx_count, 32), lambda t: (0, 0)),
            pl.BlockSpec((kyz_local, 2 * rows_pad), lambda t: (0, 0)),
            pl.BlockSpec((kyz_local, 2 * rows_pad), lambda t: (0, 0)),
        ],
        out_specs=pl.BlockSpec((1, 2, 2, kx_count, kyz_local), lambda t: (t, 0, 0, 0, 0)),
        out_shape=jax.ShapeDtypeStruct((local_frames, 2, 2, kx_count, kyz_local), jnp.float32),
        scratch_shapes=[
            pltpu.VMEM((4, rows_pad, atom_count), jnp.float32),
            pltpu.VMEM((2, 16, atom_count), jnp.float32),
            pltpu.VMEM((4, 2 * rows_pad, atom_count), jnp.bfloat16),
            pltpu.VMEM((2, 32, atom_count), jnp.bfloat16),
        ],
    )(base, onehot_all, pick_x, pick_y, pick_z)
    owned = sent_and_summed(partial_value, "atom", 3)
    densities = owned / jnp.sqrt(jnp.float32(total_atoms))
    spectra = transform(lax.all_to_all(densities, "tm", split_axis=3, concat_axis=0, tiled=True))
    return (spectra, densities)


def solution(mesh):
    in_specs = (P("tm", None, ("atom", "wave")), P("atom"), P(), P(None, "wave"))
    out_specs = (P(None, None, ("atom", "tm"), "wave"), P("tm", None, None, "atom", "wave"))
    return jax.shard_map(local, mesh=mesh, in_specs=in_specs, out_specs=out_specs, check_vma=False)
```

```python
import math

import jax
import jax.numpy as jnp
from jax import lax
from jax.experimental import pallas as pl
from jax.experimental.pallas import tpu as pltpu
from jax.sharding import PartitionSpec as P

TWO_PI = 2.0 * math.pi


def copy_for_each(shard, axis):
    peers = lax.axis_size(axis)
    return lax.all_to_all(
        jnp.broadcast_to(shard[None], (peers, *shard.shape)), axis, 0, 0, tiled=True
    )


def joined_along(pieces, dim):
    pieces = jnp.moveaxis(pieces, 0, dim)
    dims = pieces.shape
    return pieces.reshape(*dims[:dim], dims[dim] * dims[dim + 1], *dims[dim + 2 :])


def gathered_copies(shard, axis, dim):
    pieces = copy_for_each(shard, axis)
    return joined_along(pieces, dim)


def cut_along(shard, dim, peers):
    dims = shard.shape
    pieces = shard.reshape(*dims[:dim], peers, dims[dim] // peers, *dims[dim + 1 :])
    return jnp.moveaxis(pieces, dim, 0)


def sent_and_summed(shard, axis, dim):
    pieces = cut_along(shard, dim, lax.axis_size(axis))
    arrived = lax.all_to_all(pieces, axis, split_axis=0, concat_axis=0, tiled=True)
    return arrived.sum(axis=0)


def frac_turns(values):
    return values - jnp.floor(values)


def hann_window(length):
    frame_steps = jnp.arange(length).astype(jnp.float32)
    return 0.5 - 0.5 * jnp.cos(TWO_PI / length * (frame_steps + 0.5))


def combine(products):
    real_part = products[:, 0, :, 0] - products[:, 1, :, 1]
    imag_part = -(products[:, 1, :, 0] + products[:, 0, :, 1])
    return jnp.stack([real_part, imag_part], axis=1)


def transform(series, frame_of_row):
    length = series.shape[0]
    energy_window = hann_window(length)
    energy = jnp.sum(energy_window * energy_window)
    window = 0.5 - 0.5 * jnp.cos(TWO_PI / length * (frame_of_row.astype(jnp.float32) + 0.5))
    weighted = series * window[:, None, None, None, None]
    frame_steps = jnp.arange(length)
    phase_turns = (frame_steps[:, None] * frame_of_row[None, :] % length).astype(jnp.float32)
    dft_angle = TWO_PI / length * phase_turns
    cos_table = jnp.cos(dft_angle)
    sin_table = jnp.sin(dft_angle)
    real_part = weighted[:, :, 0]
    imag_part = weighted[:, :, 1]
    highest = lax.Precision.HIGHEST
    spec_real = jnp.einsum("ft,tsmj->fsmj", cos_table, real_part, precision=highest) + jnp.einsum(
        "ft,tsmj->fsmj", sin_table, imag_part, precision=highest
    )
    spec_imag = jnp.einsum("ft,tsmj->fsmj", cos_table, imag_part, precision=highest) - jnp.einsum(
        "ft,tsmj->fsmj", sin_table, real_part, precision=highest
    )
    oxygen_pair = spec_real[:, 0] * spec_real[:, 0] + spec_imag[:, 0] * spec_imag[:, 0]
    cross_pair = spec_real[:, 0] * spec_real[:, 1] + spec_imag[:, 0] * spec_imag[:, 1]
    hydrogen_pair = spec_real[:, 1] * spec_real[:, 1] + spec_imag[:, 1] * spec_imag[:, 1]
    return jnp.stack([oxygen_pair, cross_pair, hydrogen_pair]) / energy


def shifted_blocks(blocks, axis):
    peers = lax.axis_size(axis)
    me = lax.axis_index(axis)
    arrived = [lax.dynamic_index_in_dim(blocks, me, 0, keepdims=False)]
    for shift in range(1, peers):
        outgoing = lax.dynamic_index_in_dim(blocks, (me + shift) % peers, 0, keepdims=False)
        pairs = [(src, (src + shift) % peers) for src in range(peers)]
        arrived.append(lax.ppermute(outgoing, axis, pairs))
    return arrived


def power_rows(base_cos, base_sin, count):
    rows = [(jnp.ones_like(base_cos), jnp.zeros_like(base_sin)), (base_cos, base_sin)]
    for _ in range(count - 1):
        prev_cos, prev_sin = rows[-1]
        rows.append((prev_cos * base_cos - prev_sin * base_sin, prev_sin * base_cos + prev_cos * base_sin))
    return rows


def split_dot(picks, table, stacked):
    rows = table.shape[0]
    high = table.astype(jnp.bfloat16)
    stacked[0:rows, :] = high
    stacked[rows : 2 * rows, :] = (table - high.astype(jnp.float32)).astype(jnp.bfloat16)
    dims = (((1,), (0,)), ((), ()))
    return lax.dot_general(picks, stacked[...], dims, preferred_element_type=jnp.float32)


def frame_kernel(base_ref, onehot_ref, pick_x_ref, pick_y_ref, pick_z_ref, out_ref, axis_ref, x_ref, yz_half, x_half):
    base = base_ref[0]
    kmax = 16
    rows_pad = axis_ref.shape[1]
    for axis in range(2):
        powers = power_rows(base[2 + 2 * axis : 3 + 2 * axis], base[3 + 2 * axis : 4 + 2 * axis], kmax)
        for k, (cos_k, sin_k) in enumerate(powers):
            axis_ref[2 * axis, kmax + k : kmax + k + 1, :] = cos_k
            axis_ref[2 * axis + 1, kmax + k : kmax + k + 1, :] = sin_k
            if k:
                axis_ref[2 * axis, kmax - k : kmax - k + 1, :] = cos_k
                axis_ref[2 * axis + 1, kmax - k : kmax - k + 1, :] = -sin_k
        pad = rows_pad - (2 * kmax + 1)
        zeros = jnp.zeros((pad, base.shape[1]), jnp.float32)
        axis_ref[2 * axis, 2 * kmax + 1 :, :] = zeros
        axis_ref[2 * axis + 1, 2 * kmax + 1 :, :] = zeros
    x_powers = power_rows(base[0:1], base[1:2], kmax)
    for k in range(1, kmax + 1):
        x_ref[0, k - 1 : k, :] = x_powers[k][0]
        x_ref[1, k - 1 : k, :] = x_powers[k][1]
    pick_x = pick_x_ref[...]
    pick_y = pick_y_ref[...]
    pick_z = pick_z_ref[...]
    cy = split_dot(pick_y, axis_ref[0], yz_half.at[0])
    sy = split_dot(pick_y, axis_ref[1], yz_half.at[1])
    cz = split_dot(pick_z, axis_ref[2], yz_half.at[2])
    sz = split_dot(pick_z, axis_ref[3], yz_half.at[3])
    yz_cos = (cy * cz - sy * sz).astype(jnp.bfloat16)
    yz_sin = (sy * cz + cy * sz).astype(jnp.bfloat16)
    x_cos = split_dot(pick_x, x_ref[0], x_half.at[0])
    x_sin = split_dot(pick_x, x_ref[1], x_half.at[1])
    onehot = onehot_ref[...]
    x_table = jnp.concatenate(
        [onehot[0:1] * x_cos, onehot[0:1] * x_sin, onehot[1:2] * x_cos, onehot[1:2] * x_sin], axis=0
    ).astype(jnp.bfloat16)
    dims = (((1,), (1,)), ((), ()))
    with_cos = lax.dot_general(x_table, yz_cos, dims, preferred_element_type=jnp.float32)
    with_sin = lax.dot_general(x_table, yz_sin, dims, preferred_element_type=jnp.float32)
    kx = kmax
    for s in range(2):
        cos_rows = slice((2 * s) * kx, (2 * s + 1) * kx)
        sin_rows = slice((2 * s + 1) * kx, (2 * s + 2) * kx)
        out_ref[0, s, 0] = with_cos[cos_rows] - with_sin[sin_rows]
        out_ref[0, s, 1] = -(with_sin[cos_rows] + with_cos[sin_rows])


def picks_of(index, lowest, count):
    cols = jnp.arange(count, dtype=jnp.int32)
    picks = (index[:, None] - lowest == cols[None, :]).astype(jnp.bfloat16)
    return jnp.concatenate([picks, picks], axis=1)


def local(positions, species, kx_index, kyz_index):
    local_frames = positions.shape[0]
    kx_count = kx_index.shape[0]
    kyz_local = kyz_index.shape[1]
    total_atoms = positions.shape[2] * lax.axis_size("atom") * lax.axis_size("wave")
    onehot_all = jnp.stack([species == 0, species == 1]).astype(jnp.float32)
    block_coords = gathered_copies(positions, "wave", 2)
    atom_count = block_coords.shape[2]
    angle = TWO_PI * frac_turns(block_coords)
    base = jnp.stack([jnp.cos(angle), jnp.sin(angle)], axis=2).reshape(local_frames, 6, atom_count)
    rows_pad = 48
    pick_x = picks_of(kx_index, 1, 16)
    pick_y = picks_of(kyz_index[0], -16, rows_pad)
    pick_z = picks_of(kyz_index[1], -16, rows_pad)
    partial_value = pl.pallas_call(
        frame_kernel,
        grid=(local_frames,),
        in_specs=[
            pl.BlockSpec((1, 6, atom_count), lambda t: (t, 0, 0)),
            pl.BlockSpec((2, atom_count), lambda t: (0, 0)),
            pl.BlockSpec((kx_count, 32), lambda t: (0, 0)),
            pl.BlockSpec((kyz_local, 2 * rows_pad), lambda t: (0, 0)),
            pl.BlockSpec((kyz_local, 2 * rows_pad), lambda t: (0, 0)),
        ],
        out_specs=pl.BlockSpec((1, 2, 2, kx_count, kyz_local), lambda t: (t, 0, 0, 0, 0)),
        out_shape=jax.ShapeDtypeStruct((local_frames, 2, 2, kx_count, kyz_local), jnp.float32),
        scratch_shapes=[
            pltpu.VMEM((4, rows_pad, atom_count), jnp.float32),
            pltpu.VMEM((2, 16, atom_count), jnp.float32),
            pltpu.VMEM((4, 2 * rows_pad, atom_count), jnp.bfloat16),
            pltpu.VMEM((2, 32, atom_count), jnp.bfloat16),
        ],
    )(base, onehot_all, pick_x, pick_y, pick_z)
    atom_peers = lax.axis_size("atom")
    time_peers = lax.axis_size("tm")
    owned_parts = shifted_blocks(cut_along(partial_value, 3, atom_peers), "atom")
    owned = owned_parts[0]
    for part in owned_parts[1:]:
        owned = owned + part
    densities = owned / jnp.sqrt(jnp.float32(total_atoms))
    series = jnp.concatenate(shifted_blocks(cut_along(densities, 3, time_peers), "tm"), axis=0)
    me = lax.axis_index("tm")
    sources = (me - jnp.arange(time_peers)) % time_peers
    frame_of_row = (sources[:, None] * local_frames + jnp.arange(local_frames)[None, :]).reshape(-1)
    spectra = transform(series, frame_of_row)
    return (spectra, densities)


def solution(mesh):
    in_specs = (P("tm", None, ("atom", "wave")), P("atom"), P(), P(None, "wave"))
    out_specs = (P(None, None, ("atom", "tm"), "wave"), P("tm", None, None, "atom", "wave"))
    return jax.shard_map(local, mesh=mesh, in_specs=in_specs, out_specs=out_specs, check_vma=False)
```

```python
import math

import jax
import jax.numpy as jnp
from jax import lax
from jax.experimental import pallas as pl
from jax.experimental.pallas import tpu as pltpu
from jax.sharding import PartitionSpec as P

TWO_PI = 2.0 * math.pi


def copy_for_each(shard, axis):
    peers = lax.axis_size(axis)
    return lax.all_to_all(
        jnp.broadcast_to(shard[None], (peers, *shard.shape)), axis, 0, 0, tiled=True
    )


def joined_along(pieces, dim):
    pieces = jnp.moveaxis(pieces, 0, dim)
    dims = pieces.shape
    return pieces.reshape(*dims[:dim], dims[dim] * dims[dim + 1], *dims[dim + 2 :])


def gathered_copies(shard, axis, dim):
    pieces = copy_for_each(shard, axis)
    return joined_along(pieces, dim)


def cut_along(shard, dim, peers):
    dims = shard.shape
    pieces = shard.reshape(*dims[:dim], peers, dims[dim] // peers, *dims[dim + 1 :])
    return jnp.moveaxis(pieces, dim, 0)


def sent_and_summed(shard, axis, dim):
    pieces = cut_along(shard, dim, lax.axis_size(axis))
    arrived = lax.all_to_all(pieces, axis, split_axis=0, concat_axis=0, tiled=True)
    return arrived.sum(axis=0)


def frac_turns(values):
    return values - jnp.floor(values)


def hann_window(length):
    frame_steps = jnp.arange(length).astype(jnp.float32)
    return 0.5 - 0.5 * jnp.cos(TWO_PI / length * (frame_steps + 0.5))


def combine(products):
    real_part = products[:, 0, :, 0] - products[:, 1, :, 1]
    imag_part = -(products[:, 1, :, 0] + products[:, 0, :, 1])
    return jnp.stack([real_part, imag_part], axis=1)


def transform(series):
    length = series.shape[0]
    window = hann_window(length)
    energy = jnp.sum(window * window)
    weighted = series * window[:, None, None, None, None]
    frame_steps = jnp.arange(length)
    phase_turns = (frame_steps[:, None] * frame_steps[None, :] % length).astype(jnp.float32)
    dft_angle = TWO_PI / length * phase_turns
    cos_table = jnp.cos(dft_angle)
    sin_table = jnp.sin(dft_angle)
    real_part = weighted[:, :, 0]
    imag_part = weighted[:, :, 1]
    highest = lax.Precision.HIGHEST
    spec_real = jnp.einsum("ft,tsmj->fsmj", cos_table, real_part, precision=highest) + jnp.einsum(
        "ft,tsmj->fsmj", sin_table, imag_part, precision=highest
    )
    spec_imag = jnp.einsum("ft,tsmj->fsmj", cos_table, imag_part, precision=highest) - jnp.einsum(
        "ft,tsmj->fsmj", sin_table, real_part, precision=highest
    )
    oxygen_pair = spec_real[:, 0] * spec_real[:, 0] + spec_imag[:, 0] * spec_imag[:, 0]
    cross_pair = spec_real[:, 0] * spec_real[:, 1] + spec_imag[:, 0] * spec_imag[:, 1]
    hydrogen_pair = spec_real[:, 1] * spec_real[:, 1] + spec_imag[:, 1] * spec_imag[:, 1]
    return jnp.stack([oxygen_pair, cross_pair, hydrogen_pair]) / energy


def power_rows(base_cos, base_sin, count):
    rows = [(jnp.ones_like(base_cos), jnp.zeros_like(base_sin)), (base_cos, base_sin)]
    for _ in range(count - 1):
        prev_cos, prev_sin = rows[-1]
        rows.append((prev_cos * base_cos - prev_sin * base_sin, prev_sin * base_cos + prev_cos * base_sin))
    return rows


def split_dot(picks, table, stacked):
    rows = table.shape[0]
    high = table.astype(jnp.bfloat16)
    stacked[0:rows, :] = high
    stacked[rows : 2 * rows, :] = (table - high.astype(jnp.float32)).astype(jnp.bfloat16)
    dims = (((1,), (0,)), ((), ()))
    return lax.dot_general(picks, stacked[...], dims, preferred_element_type=jnp.float32)


def frame_kernel(base_ref, onehot_ref, pick_x_ref, pick_y_ref, pick_z_ref, out_ref, axis_all, x_all, yz_all, xh_all):
  for f in range(base_ref.shape[0]):
    axis_ref = axis_all.at[f]
    x_ref = x_all.at[f]
    yz_half = yz_all.at[f]
    x_half = xh_all.at[f]
    base = base_ref[f]
    kmax = 16
    rows_pad = axis_ref.shape[1]
    for axis in range(2):
        powers = power_rows(base[2 + 2 * axis : 3 + 2 * axis], base[3 + 2 * axis : 4 + 2 * axis], kmax)
        for k, (cos_k, sin_k) in enumerate(powers):
            axis_ref[2 * axis, kmax + k : kmax + k + 1, :] = cos_k
            axis_ref[2 * axis + 1, kmax + k : kmax + k + 1, :] = sin_k
            if k:
                axis_ref[2 * axis, kmax - k : kmax - k + 1, :] = cos_k
                axis_ref[2 * axis + 1, kmax - k : kmax - k + 1, :] = -sin_k
        pad = rows_pad - (2 * kmax + 1)
        zeros = jnp.zeros((pad, base.shape[1]), jnp.float32)
        axis_ref[2 * axis, 2 * kmax + 1 :, :] = zeros
        axis_ref[2 * axis + 1, 2 * kmax + 1 :, :] = zeros
    x_powers = power_rows(base[0:1], base[1:2], kmax)
    for k in range(1, kmax + 1):
        x_ref[0, k - 1 : k, :] = x_powers[k][0]
        x_ref[1, k - 1 : k, :] = x_powers[k][1]
    pick_x = pick_x_ref[...]
    pick_y = pick_y_ref[...]
    pick_z = pick_z_ref[...]
    cy = split_dot(pick_y, axis_ref[0], yz_half.at[0])
    sy = split_dot(pick_y, axis_ref[1], yz_half.at[1])
    cz = split_dot(pick_z, axis_ref[2], yz_half.at[2])
    sz = split_dot(pick_z, axis_ref[3], yz_half.at[3])
    yz_cos = (cy * cz - sy * sz).astype(jnp.bfloat16)
    yz_sin = (sy * cz + cy * sz).astype(jnp.bfloat16)
    x_cos = split_dot(pick_x, x_ref[0], x_half.at[0])
    x_sin = split_dot(pick_x, x_ref[1], x_half.at[1])
    onehot = onehot_ref[...]
    x_table = jnp.concatenate(
        [onehot[0:1] * x_cos, onehot[0:1] * x_sin, onehot[1:2] * x_cos, onehot[1:2] * x_sin], axis=0
    ).astype(jnp.bfloat16)
    dims = (((1,), (1,)), ((), ()))
    with_cos = lax.dot_general(x_table, yz_cos, dims, preferred_element_type=jnp.float32)
    with_sin = lax.dot_general(x_table, yz_sin, dims, preferred_element_type=jnp.float32)
    kx = kmax
    for s in range(2):
        cos_rows = slice((2 * s) * kx, (2 * s + 1) * kx)
        sin_rows = slice((2 * s + 1) * kx, (2 * s + 2) * kx)
        out_ref[f, s, 0] = with_cos[cos_rows] - with_sin[sin_rows]
        out_ref[f, s, 1] = -(with_sin[cos_rows] + with_cos[sin_rows])


def picks_of(index, lowest, count):
    cols = jnp.arange(count, dtype=jnp.int32)
    picks = (index[:, None] - lowest == cols[None, :]).astype(jnp.bfloat16)
    return jnp.concatenate([picks, picks], axis=1)


def local(positions, species, kx_index, kyz_index):
    local_frames = positions.shape[0]
    kx_count = kx_index.shape[0]
    kyz_local = kyz_index.shape[1]
    total_atoms = positions.shape[2] * lax.axis_size("atom") * lax.axis_size("wave")
    onehot_all = jnp.stack([species == 0, species == 1]).astype(jnp.float32)
    block_coords = gathered_copies(positions, "wave", 2)
    atom_count = block_coords.shape[2]
    angle = TWO_PI * frac_turns(block_coords)
    base = jnp.stack([jnp.cos(angle), jnp.sin(angle)], axis=2).reshape(local_frames, 6, atom_count)
    rows_pad = 48
    frames_per_step = math.gcd(local_frames, 4)
    pick_x = picks_of(kx_index, 1, 16)
    pick_y = picks_of(kyz_index[0], -16, rows_pad)
    pick_z = picks_of(kyz_index[1], -16, rows_pad)
    partial_value = pl.pallas_call(
        frame_kernel,
        grid=(local_frames // frames_per_step,),
        in_specs=[
            pl.BlockSpec((frames_per_step, 6, atom_count), lambda t: (t, 0, 0)),
            pl.BlockSpec((2, atom_count), lambda t: (0, 0)),
            pl.BlockSpec((kx_count, 32), lambda t: (0, 0)),
            pl.BlockSpec((kyz_local, 2 * rows_pad), lambda t: (0, 0)),
            pl.BlockSpec((kyz_local, 2 * rows_pad), lambda t: (0, 0)),
        ],
        out_specs=pl.BlockSpec((frames_per_step, 2, 2, kx_count, kyz_local), lambda t: (t, 0, 0, 0, 0)),
        out_shape=jax.ShapeDtypeStruct((local_frames, 2, 2, kx_count, kyz_local), jnp.float32),
        scratch_shapes=[
            pltpu.VMEM((frames_per_step, 4, rows_pad, atom_count), jnp.float32),
            pltpu.VMEM((frames_per_step, 2, 16, atom_count), jnp.float32),
            pltpu.VMEM((frames_per_step, 4, 2 * rows_pad, atom_count), jnp.bfloat16),
            pltpu.VMEM((frames_per_step, 2, 32, atom_count), jnp.bfloat16),
        ],
    )(base, onehot_all, pick_x, pick_y, pick_z)
    owned = sent_and_summed(partial_value, "atom", 3)
    densities = owned / jnp.sqrt(jnp.float32(total_atoms))
    spectra = transform(lax.all_to_all(densities, "tm", split_axis=3, concat_axis=0, tiled=True))
    return (spectra, densities)


def solution(mesh):
    in_specs = (P("tm", None, ("atom", "wave")), P("atom"), P(), P(None, "wave"))
    out_specs = (P(None, None, ("atom", "tm"), "wave"), P("tm", None, None, "atom", "wave"))
    return jax.shard_map(local, mesh=mesh, in_specs=in_specs, out_specs=out_specs, check_vma=False)
```

```python
import math

import jax
import jax.numpy as jnp
from jax import lax
from jax.experimental import pallas as pl
from jax.experimental.pallas import tpu as pltpu
from jax.sharding import PartitionSpec as P

TWO_PI = 2.0 * math.pi


def copy_for_each(shard, axis):
    peers = lax.axis_size(axis)
    return lax.all_to_all(
        jnp.broadcast_to(shard[None], (peers, *shard.shape)), axis, 0, 0, tiled=True
    )


def joined_along(pieces, dim):
    pieces = jnp.moveaxis(pieces, 0, dim)
    dims = pieces.shape
    return pieces.reshape(*dims[:dim], dims[dim] * dims[dim + 1], *dims[dim + 2 :])


def gathered_copies(shard, axis, dim):
    pieces = copy_for_each(shard, axis)
    return joined_along(pieces, dim)


def cut_along(shard, dim, peers):
    dims = shard.shape
    pieces = shard.reshape(*dims[:dim], peers, dims[dim] // peers, *dims[dim + 1 :])
    return jnp.moveaxis(pieces, dim, 0)


def sent_and_summed(shard, axis, dim):
    pieces = cut_along(shard, dim, lax.axis_size(axis))
    arrived = lax.all_to_all(pieces, axis, split_axis=0, concat_axis=0, tiled=True)
    return arrived.sum(axis=0)


def frac_turns(values):
    return values - jnp.floor(values)


def hann_window(length):
    frame_steps = jnp.arange(length).astype(jnp.float32)
    return 0.5 - 0.5 * jnp.cos(TWO_PI / length * (frame_steps + 0.5))


def combine(products):
    real_part = products[:, 0, :, 0] - products[:, 1, :, 1]
    imag_part = -(products[:, 1, :, 0] + products[:, 0, :, 1])
    return jnp.stack([real_part, imag_part], axis=1)


def transform(series):
    length = series.shape[0]
    window = hann_window(length)
    energy = jnp.sum(window * window)
    weighted = series * window[:, None, None, None, None]
    frame_steps = jnp.arange(length)
    phase_turns = (frame_steps[:, None] * frame_steps[None, :] % length).astype(jnp.float32)
    dft_angle = TWO_PI / length * phase_turns
    cos_table = jnp.cos(dft_angle)
    sin_table = jnp.sin(dft_angle)
    real_part = weighted[:, :, 0]
    imag_part = weighted[:, :, 1]
    highest = lax.Precision.HIGHEST
    spec_real = jnp.einsum("ft,tsmj->fsmj", cos_table, real_part, precision=highest) + jnp.einsum(
        "ft,tsmj->fsmj", sin_table, imag_part, precision=highest
    )
    spec_imag = jnp.einsum("ft,tsmj->fsmj", cos_table, imag_part, precision=highest) - jnp.einsum(
        "ft,tsmj->fsmj", sin_table, real_part, precision=highest
    )
    oxygen_pair = spec_real[:, 0] * spec_real[:, 0] + spec_imag[:, 0] * spec_imag[:, 0]
    cross_pair = spec_real[:, 0] * spec_real[:, 1] + spec_imag[:, 0] * spec_imag[:, 1]
    hydrogen_pair = spec_real[:, 1] * spec_real[:, 1] + spec_imag[:, 1] * spec_imag[:, 1]
    return jnp.stack([oxygen_pair, cross_pair, hydrogen_pair]) / energy


def power_rows(base_cos, base_sin, count):
    rows = [(jnp.ones_like(base_cos), jnp.zeros_like(base_sin)), (base_cos, base_sin)]
    for _ in range(count - 1):
        prev_cos, prev_sin = rows[-1]
        rows.append((prev_cos * base_cos - prev_sin * base_sin, prev_sin * base_cos + prev_cos * base_sin))
    return rows


def split_dot(picks, table, stacked):
    rows = table.shape[0]
    high = table.astype(jnp.bfloat16)
    stacked[0:rows, :] = high
    stacked[rows : 2 * rows, :] = (table - high.astype(jnp.float32)).astype(jnp.bfloat16)
    dims = (((1,), (0,)), ((), ()))
    return lax.dot_general(picks, stacked[...], dims, preferred_element_type=jnp.float32)


def frame_kernel(base_ref, onehot_ref, pick_x_ref, pick_y_ref, pick_z_ref, out_ref, axis_all, x_all, yz_all, xh_all):
  for f in range(base_ref.shape[0]):
    axis_ref = axis_all.at[f]
    x_ref = x_all.at[f]
    yz_half = yz_all.at[f]
    x_half = xh_all.at[f]
    base = base_ref[f]
    kmax = 16
    rows_pad = axis_ref.shape[1]
    for axis in range(2):
        powers = power_rows(base[2 + 2 * axis : 3 + 2 * axis], base[3 + 2 * axis : 4 + 2 * axis], kmax)
        for k, (cos_k, sin_k) in enumerate(powers):
            axis_ref[2 * axis, kmax + k : kmax + k + 1, :] = cos_k
            axis_ref[2 * axis + 1, kmax + k : kmax + k + 1, :] = sin_k
            if k:
                axis_ref[2 * axis, kmax - k : kmax - k + 1, :] = cos_k
                axis_ref[2 * axis + 1, kmax - k : kmax - k + 1, :] = -sin_k
        pad = rows_pad - (2 * kmax + 1)
        zeros = jnp.zeros((pad, base.shape[1]), jnp.float32)
        axis_ref[2 * axis, 2 * kmax + 1 :, :] = zeros
        axis_ref[2 * axis + 1, 2 * kmax + 1 :, :] = zeros
    x_powers = power_rows(base[0:1], base[1:2], kmax)
    for k in range(1, kmax + 1):
        x_ref[0, k - 1 : k, :] = x_powers[k][0]
        x_ref[1, k - 1 : k, :] = x_powers[k][1]
    pick_x = pick_x_ref[...]
    pick_y = pick_y_ref[...]
    pick_z = pick_z_ref[...]
    cy = split_dot(pick_y, axis_ref[0], yz_half.at[0])
    sy = split_dot(pick_y, axis_ref[1], yz_half.at[1])
    cz = split_dot(pick_z, axis_ref[2], yz_half.at[2])
    sz = split_dot(pick_z, axis_ref[3], yz_half.at[3])
    yz_cos = (cy * cz - sy * sz).astype(jnp.bfloat16)
    yz_sin = (sy * cz + cy * sz).astype(jnp.bfloat16)
    x_cos = split_dot(pick_x, x_ref[0], x_half.at[0])
    x_sin = split_dot(pick_x, x_ref[1], x_half.at[1])
    onehot = onehot_ref[...]
    x_table = jnp.concatenate(
        [onehot[0:1] * x_cos, onehot[0:1] * x_sin, onehot[1:2] * x_cos, onehot[1:2] * x_sin], axis=0
    ).astype(jnp.bfloat16)
    dims = (((1,), (1,)), ((), ()))
    with_cos = lax.dot_general(x_table, yz_cos, dims, preferred_element_type=jnp.float32)
    with_sin = lax.dot_general(x_table, yz_sin, dims, preferred_element_type=jnp.float32)
    kx = kmax
    for s in range(2):
        cos_rows = slice((2 * s) * kx, (2 * s + 1) * kx)
        sin_rows = slice((2 * s + 1) * kx, (2 * s + 2) * kx)
        out_ref[f, s, 0] = with_cos[cos_rows] - with_sin[sin_rows]
        out_ref[f, s, 1] = -(with_sin[cos_rows] + with_cos[sin_rows])


def picks_of(index, lowest, count):
    cols = jnp.arange(count, dtype=jnp.int32)
    picks = (index[:, None] - lowest == cols[None, :]).astype(jnp.bfloat16)
    return jnp.concatenate([picks, picks], axis=1)


def local(positions, species, kx_index, kyz_index):
    local_frames = positions.shape[0]
    kx_count = kx_index.shape[0]
    kyz_local = kyz_index.shape[1]
    total_atoms = positions.shape[2] * lax.axis_size("atom") * lax.axis_size("wave")
    onehot_all = jnp.stack([species == 0, species == 1]).astype(jnp.float32)
    block_coords = gathered_copies(positions, "wave", 2)
    atom_count = block_coords.shape[2]
    angle = TWO_PI * frac_turns(block_coords)
    base = jnp.stack([jnp.cos(angle), jnp.sin(angle)], axis=2).reshape(local_frames, 6, atom_count)
    rows_pad = 48
    frames_per_step = math.gcd(local_frames, 8)
    pick_x = picks_of(kx_index, 1, 16)
    pick_y = picks_of(kyz_index[0], -16, rows_pad)
    pick_z = picks_of(kyz_index[1], -16, rows_pad)
    partial_value = pl.pallas_call(
        frame_kernel,
        grid=(local_frames // frames_per_step,),
        in_specs=[
            pl.BlockSpec((frames_per_step, 6, atom_count), lambda t: (t, 0, 0)),
            pl.BlockSpec((2, atom_count), lambda t: (0, 0)),
            pl.BlockSpec((kx_count, 32), lambda t: (0, 0)),
            pl.BlockSpec((kyz_local, 2 * rows_pad), lambda t: (0, 0)),
            pl.BlockSpec((kyz_local, 2 * rows_pad), lambda t: (0, 0)),
        ],
        out_specs=pl.BlockSpec((frames_per_step, 2, 2, kx_count, kyz_local), lambda t: (t, 0, 0, 0, 0)),
        out_shape=jax.ShapeDtypeStruct((local_frames, 2, 2, kx_count, kyz_local), jnp.float32),
        scratch_shapes=[
            pltpu.VMEM((frames_per_step, 4, rows_pad, atom_count), jnp.float32),
            pltpu.VMEM((frames_per_step, 2, 16, atom_count), jnp.float32),
            pltpu.VMEM((frames_per_step, 4, 2 * rows_pad, atom_count), jnp.bfloat16),
            pltpu.VMEM((frames_per_step, 2, 32, atom_count), jnp.bfloat16),
        ],
    )(base, onehot_all, pick_x, pick_y, pick_z)
    owned = sent_and_summed(partial_value, "atom", 3)
    densities = owned / jnp.sqrt(jnp.float32(total_atoms))
    spectra = transform(lax.all_to_all(densities, "tm", split_axis=3, concat_axis=0, tiled=True))
    return (spectra, densities)


def solution(mesh):
    in_specs = (P("tm", None, ("atom", "wave")), P("atom"), P(), P(None, "wave"))
    out_specs = (P(None, None, ("atom", "tm"), "wave"), P("tm", None, None, "atom", "wave"))
    return jax.shard_map(local, mesh=mesh, in_specs=in_specs, out_specs=out_specs, check_vma=False)
```

```python
import math

import jax
import jax.numpy as jnp
from jax import lax
from jax.experimental import pallas as pl
from jax.experimental.pallas import tpu as pltpu
from jax.sharding import PartitionSpec as P

TWO_PI = 2.0 * math.pi


def copy_for_each(shard, axis):
    peers = lax.axis_size(axis)
    return lax.all_to_all(
        jnp.broadcast_to(shard[None], (peers, *shard.shape)), axis, 0, 0, tiled=True
    )


def joined_along(pieces, dim):
    pieces = jnp.moveaxis(pieces, 0, dim)
    dims = pieces.shape
    return pieces.reshape(*dims[:dim], dims[dim] * dims[dim + 1], *dims[dim + 2 :])


def gathered_copies(shard, axis, dim):
    pieces = copy_for_each(shard, axis)
    return joined_along(pieces, dim)


def cut_along(shard, dim, peers):
    dims = shard.shape
    pieces = shard.reshape(*dims[:dim], peers, dims[dim] // peers, *dims[dim + 1 :])
    return jnp.moveaxis(pieces, dim, 0)


def sent_and_summed(shard, axis, dim):
    pieces = cut_along(shard, dim, lax.axis_size(axis))
    arrived = lax.all_to_all(pieces, axis, split_axis=0, concat_axis=0, tiled=True)
    return arrived.sum(axis=0)


def frac_turns(values):
    return values - jnp.floor(values)


def hann_window(length):
    frame_steps = jnp.arange(length).astype(jnp.float32)
    return 0.5 - 0.5 * jnp.cos(TWO_PI / length * (frame_steps + 0.5))


def combine(products):
    real_part = products[:, 0, :, 0] - products[:, 1, :, 1]
    imag_part = -(products[:, 1, :, 0] + products[:, 0, :, 1])
    return jnp.stack([real_part, imag_part], axis=1)


def transform(series):
    length = series.shape[0]
    window = hann_window(length)
    energy = jnp.sum(window * window)
    weighted = series * window[:, None, None, None, None]
    frame_steps = jnp.arange(length)
    phase_turns = (frame_steps[:, None] * frame_steps[None, :] % length).astype(jnp.float32)
    dft_angle = TWO_PI / length * phase_turns
    cos_table = jnp.cos(dft_angle)
    sin_table = jnp.sin(dft_angle)
    real_part = weighted[:, :, 0]
    imag_part = weighted[:, :, 1]
    highest = lax.Precision.HIGHEST
    spec_real = jnp.einsum("ft,tsmj->fsmj", cos_table, real_part, precision=highest) + jnp.einsum(
        "ft,tsmj->fsmj", sin_table, imag_part, precision=highest
    )
    spec_imag = jnp.einsum("ft,tsmj->fsmj", cos_table, imag_part, precision=highest) - jnp.einsum(
        "ft,tsmj->fsmj", sin_table, real_part, precision=highest
    )
    oxygen_pair = spec_real[:, 0] * spec_real[:, 0] + spec_imag[:, 0] * spec_imag[:, 0]
    cross_pair = spec_real[:, 0] * spec_real[:, 1] + spec_imag[:, 0] * spec_imag[:, 1]
    hydrogen_pair = spec_real[:, 1] * spec_real[:, 1] + spec_imag[:, 1] * spec_imag[:, 1]
    return jnp.stack([oxygen_pair, cross_pair, hydrogen_pair]) / energy


def power_rows(base_cos, base_sin, count):
    rows = [(jnp.ones_like(base_cos), jnp.zeros_like(base_sin)), (base_cos, base_sin)]
    for _ in range(count - 1):
        prev_cos, prev_sin = rows[-1]
        rows.append((prev_cos * base_cos - prev_sin * base_sin, prev_sin * base_cos + prev_cos * base_sin))
    return rows


def split_dot(picks, table, stacked):
    rows = table.shape[0]
    high = table.astype(jnp.bfloat16)
    stacked[0:rows, :] = high
    stacked[rows : 2 * rows, :] = (table - high.astype(jnp.float32)).astype(jnp.bfloat16)
    dims = (((1,), (0,)), ((), ()))
    return lax.dot_general(picks, stacked[...], dims, preferred_element_type=jnp.float32)


def frame_kernel(base_ref, onehot_ref, pick_x_ref, pick_y_ref, pick_z_ref, out_ref, axis_all, x_all, yz_all, xh_all):
  for f in range(base_ref.shape[0]):
    axis_ref = axis_all.at[f]
    x_ref = x_all.at[f]
    yz_half = yz_all.at[f]
    x_half = xh_all.at[f]
    base = base_ref[f]
    kmax = 16
    rows_pad = axis_ref.shape[1]
    for axis in range(2):
        powers = power_rows(base[2 + 2 * axis : 3 + 2 * axis], base[3 + 2 * axis : 4 + 2 * axis], kmax)
        for k, (cos_k, sin_k) in enumerate(powers):
            axis_ref[2 * axis, kmax + k : kmax + k + 1, :] = cos_k
            axis_ref[2 * axis + 1, kmax + k : kmax + k + 1, :] = sin_k
            if k:
                axis_ref[2 * axis, kmax - k : kmax - k + 1, :] = cos_k
                axis_ref[2 * axis + 1, kmax - k : kmax - k + 1, :] = -sin_k
        pad = rows_pad - (2 * kmax + 1)
        zeros = jnp.zeros((pad, base.shape[1]), jnp.float32)
        axis_ref[2 * axis, 2 * kmax + 1 :, :] = zeros
        axis_ref[2 * axis + 1, 2 * kmax + 1 :, :] = zeros
    x_powers = power_rows(base[0:1], base[1:2], kmax)
    for k in range(1, kmax + 1):
        x_ref[0, k - 1 : k, :] = x_powers[k][0]
        x_ref[1, k - 1 : k, :] = x_powers[k][1]
    pick_x = pick_x_ref[...]
    pick_y = pick_y_ref[...]
    pick_z = pick_z_ref[...]
    cy = split_dot(pick_y, axis_ref[0], yz_half.at[0])
    sy = split_dot(pick_y, axis_ref[1], yz_half.at[1])
    cz = split_dot(pick_z, axis_ref[2], yz_half.at[2])
    sz = split_dot(pick_z, axis_ref[3], yz_half.at[3])
    yz_cos = (cy * cz - sy * sz).astype(jnp.bfloat16)
    yz_sin = (sy * cz + cy * sz).astype(jnp.bfloat16)
    x_cos = split_dot(pick_x, x_ref[0], x_half.at[0])
    x_sin = split_dot(pick_x, x_ref[1], x_half.at[1])
    onehot = onehot_ref[...]
    x_table = jnp.concatenate(
        [onehot[0:1] * x_cos, onehot[0:1] * x_sin, onehot[1:2] * x_cos, onehot[1:2] * x_sin], axis=0
    ).astype(jnp.bfloat16)
    dims = (((1,), (1,)), ((), ()))
    with_cos = lax.dot_general(x_table, yz_cos, dims, preferred_element_type=jnp.float32)
    with_sin = lax.dot_general(x_table, yz_sin, dims, preferred_element_type=jnp.float32)
    kx = kmax
    for s in range(2):
        cos_rows = slice((2 * s) * kx, (2 * s + 1) * kx)
        sin_rows = slice((2 * s + 1) * kx, (2 * s + 2) * kx)
        out_ref[f, s, 0] = with_cos[cos_rows] - with_sin[sin_rows]
        out_ref[f, s, 1] = -(with_sin[cos_rows] + with_cos[sin_rows])


def picks_of(index, lowest, count):
    cols = jnp.arange(count, dtype=jnp.int32)
    picks = (index[:, None] - lowest == cols[None, :]).astype(jnp.bfloat16)
    return jnp.concatenate([picks, picks], axis=1)


def local(positions, species, kx_index, kyz_index):
    local_frames = positions.shape[0]
    kx_count = kx_index.shape[0]
    kyz_local = kyz_index.shape[1]
    total_atoms = positions.shape[2] * lax.axis_size("atom") * lax.axis_size("wave")
    onehot_all = jnp.stack([species == 0, species == 1]).astype(jnp.float32)
    angle = TWO_PI * frac_turns(positions)
    local_base = jnp.stack([jnp.cos(angle), jnp.sin(angle)], axis=2).reshape(local_frames, 6, positions.shape[2])
    base = gathered_copies(local_base, "wave", 2)
    atom_count = base.shape[2]
    rows_pad = 48
    frames_per_step = math.gcd(local_frames, 8)
    pick_x = picks_of(kx_index, 1, 16)
    pick_y = picks_of(kyz_index[0], -16, rows_pad)
    pick_z = picks_of(kyz_index[1], -16, rows_pad)
    partial_value = pl.pallas_call(
        frame_kernel,
        grid=(local_frames // frames_per_step,),
        in_specs=[
            pl.BlockSpec((frames_per_step, 6, atom_count), lambda t: (t, 0, 0)),
            pl.BlockSpec((2, atom_count), lambda t: (0, 0)),
            pl.BlockSpec((kx_count, 32), lambda t: (0, 0)),
            pl.BlockSpec((kyz_local, 2 * rows_pad), lambda t: (0, 0)),
            pl.BlockSpec((kyz_local, 2 * rows_pad), lambda t: (0, 0)),
        ],
        out_specs=pl.BlockSpec((frames_per_step, 2, 2, kx_count, kyz_local), lambda t: (t, 0, 0, 0, 0)),
        out_shape=jax.ShapeDtypeStruct((local_frames, 2, 2, kx_count, kyz_local), jnp.float32),
        scratch_shapes=[
            pltpu.VMEM((frames_per_step, 4, rows_pad, atom_count), jnp.float32),
            pltpu.VMEM((frames_per_step, 2, 16, atom_count), jnp.float32),
            pltpu.VMEM((frames_per_step, 4, 2 * rows_pad, atom_count), jnp.bfloat16),
            pltpu.VMEM((frames_per_step, 2, 32, atom_count), jnp.bfloat16),
        ],
    )(base, onehot_all, pick_x, pick_y, pick_z)
    owned = sent_and_summed(partial_value, "atom", 3)
    densities = owned / jnp.sqrt(jnp.float32(total_atoms))
    spectra = transform(lax.all_to_all(densities, "tm", split_axis=3, concat_axis=0, tiled=True))
    return (spectra, densities)


def solution(mesh):
    in_specs = (P("tm", None, ("atom", "wave")), P("atom"), P(), P(None, "wave"))
    out_specs = (P(None, None, ("atom", "tm"), "wave"), P("tm", None, None, "atom", "wave"))
    return jax.shard_map(local, mesh=mesh, in_specs=in_specs, out_specs=out_specs, check_vma=False)
```

```python
import math

import jax
import jax.numpy as jnp
from jax import lax
from jax.experimental import pallas as pl
from jax.experimental.pallas import tpu as pltpu
from jax.sharding import PartitionSpec as P

TWO_PI = 2.0 * math.pi


def copy_for_each(shard, axis):
    peers = lax.axis_size(axis)
    return lax.all_to_all(
        jnp.broadcast_to(shard[None], (peers, *shard.shape)), axis, 0, 0, tiled=True
    )


def joined_along(pieces, dim):
    pieces = jnp.moveaxis(pieces, 0, dim)
    dims = pieces.shape
    return pieces.reshape(*dims[:dim], dims[dim] * dims[dim + 1], *dims[dim + 2 :])


def gathered_copies(shard, axis, dim):
    pieces = copy_for_each(shard, axis)
    return joined_along(pieces, dim)


def cut_along(shard, dim, peers):
    dims = shard.shape
    pieces = shard.reshape(*dims[:dim], peers, dims[dim] // peers, *dims[dim + 1 :])
    return jnp.moveaxis(pieces, dim, 0)


def sent_and_summed(shard, axis, dim):
    pieces = cut_along(shard, dim, lax.axis_size(axis))
    arrived = lax.all_to_all(pieces, axis, split_axis=0, concat_axis=0, tiled=True)
    return arrived.sum(axis=0)


def frac_turns(values):
    return values - jnp.floor(values)


def hann_window(length):
    frame_steps = jnp.arange(length).astype(jnp.float32)
    return 0.5 - 0.5 * jnp.cos(TWO_PI / length * (frame_steps + 0.5))


def combine(products):
    real_part = products[:, 0, :, 0] - products[:, 1, :, 1]
    imag_part = -(products[:, 1, :, 0] + products[:, 0, :, 1])
    return jnp.stack([real_part, imag_part], axis=1)


def transform(series):
    length = series.shape[0]
    window = hann_window(length)
    energy = jnp.sum(window * window)
    weighted = series * window[:, None, None, None, None]
    frame_steps = jnp.arange(length)
    phase_turns = (frame_steps[:, None] * frame_steps[None, :] % length).astype(jnp.float32)
    dft_angle = TWO_PI / length * phase_turns
    cos_table = jnp.cos(dft_angle)
    sin_table = jnp.sin(dft_angle)
    real_part = weighted[:, :, 0]
    imag_part = weighted[:, :, 1]
    highest = lax.Precision.HIGHEST
    spec_real = jnp.einsum("ft,tsmj->fsmj", cos_table, real_part, precision=highest) + jnp.einsum(
        "ft,tsmj->fsmj", sin_table, imag_part, precision=highest
    )
    spec_imag = jnp.einsum("ft,tsmj->fsmj", cos_table, imag_part, precision=highest) - jnp.einsum(
        "ft,tsmj->fsmj", sin_table, real_part, precision=highest
    )
    oxygen_pair = spec_real[:, 0] * spec_real[:, 0] + spec_imag[:, 0] * spec_imag[:, 0]
    cross_pair = spec_real[:, 0] * spec_real[:, 1] + spec_imag[:, 0] * spec_imag[:, 1]
    hydrogen_pair = spec_real[:, 1] * spec_real[:, 1] + spec_imag[:, 1] * spec_imag[:, 1]
    return jnp.stack([oxygen_pair, cross_pair, hydrogen_pair]) / energy


def power_rows(base_cos, base_sin, count):
    rows = [(jnp.ones_like(base_cos), jnp.zeros_like(base_sin)), (base_cos, base_sin)]
    for _ in range(count - 1):
        prev_cos, prev_sin = rows[-1]
        rows.append((prev_cos * base_cos - prev_sin * base_sin, prev_sin * base_cos + prev_cos * base_sin))
    return rows


def split_dot(picks, table, stacked):
    rows = table.shape[0]
    high = table.astype(jnp.bfloat16)
    stacked[0:rows, :] = high
    stacked[rows : 2 * rows, :] = (table - high.astype(jnp.float32)).astype(jnp.bfloat16)
    dims = (((1,), (0,)), ((), ()))
    return lax.dot_general(picks, stacked[...], dims, preferred_element_type=jnp.float32)


def frame_kernel(base_ref, onehot_ref, pick_x_ref, pick_y_ref, pick_z_ref, out_ref, axis_all, x_all, yz_all, xh_all):
  for f in range(base_ref.shape[0]):
    axis_ref = axis_all.at[f]
    x_ref = x_all.at[f]
    yz_half = yz_all.at[f]
    x_half = xh_all.at[f]
    base = base_ref[f]
    kmax = 16
    rows_pad = axis_ref.shape[1]
    for axis in range(2):
        powers = power_rows(base[2 + 2 * axis : 3 + 2 * axis], base[3 + 2 * axis : 4 + 2 * axis], kmax)
        for k, (cos_k, sin_k) in enumerate(powers):
            axis_ref[2 * axis, kmax + k : kmax + k + 1, :] = cos_k
            axis_ref[2 * axis + 1, kmax + k : kmax + k + 1, :] = sin_k
            if k:
                axis_ref[2 * axis, kmax - k : kmax - k + 1, :] = cos_k
                axis_ref[2 * axis + 1, kmax - k : kmax - k + 1, :] = -sin_k
        pad = rows_pad - (2 * kmax + 1)
        zeros = jnp.zeros((pad, base.shape[1]), jnp.float32)
        axis_ref[2 * axis, 2 * kmax + 1 :, :] = zeros
        axis_ref[2 * axis + 1, 2 * kmax + 1 :, :] = zeros
    x_powers = power_rows(base[0:1], base[1:2], kmax)
    for k in range(1, kmax + 1):
        x_ref[0, k - 1 : k, :] = x_powers[k][0]
        x_ref[1, k - 1 : k, :] = x_powers[k][1]
    pick_x = pick_x_ref[...]
    pick_y = pick_y_ref[...]
    pick_z = pick_z_ref[...]
    cy = split_dot(pick_y, axis_ref[0], yz_half.at[0])
    sy = split_dot(pick_y, axis_ref[1], yz_half.at[1])
    cz = split_dot(pick_z, axis_ref[2], yz_half.at[2])
    sz = split_dot(pick_z, axis_ref[3], yz_half.at[3])
    yz_cos = (cy * cz - sy * sz).astype(jnp.bfloat16)
    yz_sin = (sy * cz + cy * sz).astype(jnp.bfloat16)
    x_cos = split_dot(pick_x, x_ref[0], x_half.at[0])
    x_sin = split_dot(pick_x, x_ref[1], x_half.at[1])
    onehot = onehot_ref[...]
    x_table = jnp.concatenate(
        [onehot[0:1] * x_cos, onehot[0:1] * x_sin, onehot[1:2] * x_cos, onehot[1:2] * x_sin], axis=0
    ).astype(jnp.bfloat16)
    dims = (((1,), (1,)), ((), ()))
    with_cos = lax.dot_general(x_table, yz_cos, dims, preferred_element_type=jnp.float32)
    with_sin = lax.dot_general(x_table, yz_sin, dims, preferred_element_type=jnp.float32)
    kx = kmax
    for s in range(2):
        cos_rows = slice((2 * s) * kx, (2 * s + 1) * kx)
        sin_rows = slice((2 * s + 1) * kx, (2 * s + 2) * kx)
        out_ref[f, s, 0] = with_cos[cos_rows] - with_sin[sin_rows]
        out_ref[f, s, 1] = -(with_sin[cos_rows] + with_cos[sin_rows])


def picks_of(index, lowest, count):
    cols = jnp.arange(count, dtype=jnp.int32)
    picks = (index[:, None] - lowest == cols[None, :]).astype(jnp.bfloat16)
    return jnp.concatenate([picks, picks], axis=1)


def local(positions, species, kx_index, kyz_index):
    local_frames = positions.shape[0]
    kx_count = kx_index.shape[0]
    kyz_local = kyz_index.shape[1]
    total_atoms = positions.shape[2] * lax.axis_size("atom") * lax.axis_size("wave")
    onehot_all = jnp.stack([species == 0, species == 1]).astype(jnp.float32)
    flat = positions.size
    lane_rows = flat // 128 if flat % 128 == 0 else 1
    packed = copy_for_each(positions.reshape(lane_rows, flat // lane_rows), "wave")
    peers = lax.axis_size("wave")
    block_coords = joined_along(packed.reshape(peers, *positions.shape), 2)
    atom_count = block_coords.shape[2]
    angle = TWO_PI * frac_turns(block_coords)
    base = jnp.stack([jnp.cos(angle), jnp.sin(angle)], axis=2).reshape(local_frames, 6, atom_count)
    rows_pad = 48
    frames_per_step = math.gcd(local_frames, 8)
    pick_x = picks_of(kx_index, 1, 16)
    pick_y = picks_of(kyz_index[0], -16, rows_pad)
    pick_z = picks_of(kyz_index[1], -16, rows_pad)
    partial_value = pl.pallas_call(
        frame_kernel,
        grid=(local_frames // frames_per_step,),
        in_specs=[
            pl.BlockSpec((frames_per_step, 6, atom_count), lambda t: (t, 0, 0)),
            pl.BlockSpec((2, atom_count), lambda t: (0, 0)),
            pl.BlockSpec((kx_count, 32), lambda t: (0, 0)),
            pl.BlockSpec((kyz_local, 2 * rows_pad), lambda t: (0, 0)),
            pl.BlockSpec((kyz_local, 2 * rows_pad), lambda t: (0, 0)),
        ],
        out_specs=pl.BlockSpec((frames_per_step, 2, 2, kx_count, kyz_local), lambda t: (t, 0, 0, 0, 0)),
        out_shape=jax.ShapeDtypeStruct((local_frames, 2, 2, kx_count, kyz_local), jnp.float32),
        scratch_shapes=[
            pltpu.VMEM((frames_per_step, 4, rows_pad, atom_count), jnp.float32),
            pltpu.VMEM((frames_per_step, 2, 16, atom_count), jnp.float32),
            pltpu.VMEM((frames_per_step, 4, 2 * rows_pad, atom_count), jnp.bfloat16),
            pltpu.VMEM((frames_per_step, 2, 32, atom_count), jnp.bfloat16),
        ],
    )(base, onehot_all, pick_x, pick_y, pick_z)
    owned = sent_and_summed(partial_value, "atom", 3)
    densities = owned / jnp.sqrt(jnp.float32(total_atoms))
    spectra = transform(lax.all_to_all(densities, "tm", split_axis=3, concat_axis=0, tiled=True))
    return (spectra, densities)


def solution(mesh):
    in_specs = (P("tm", None, ("atom", "wave")), P("atom"), P(), P(None, "wave"))
    out_specs = (P(None, None, ("atom", "tm"), "wave"), P("tm", None, None, "atom", "wave"))
    return jax.shard_map(local, mesh=mesh, in_specs=in_specs, out_specs=out_specs, check_vma=False)
```

```python
import math

import jax
import jax.numpy as jnp
from jax import lax
from jax.experimental import pallas as pl
from jax.experimental.pallas import tpu as pltpu
from jax.sharding import PartitionSpec as P

TWO_PI = 2.0 * math.pi


def copy_for_each(shard, axis):
    peers = lax.axis_size(axis)
    return lax.all_to_all(
        jnp.broadcast_to(shard[None], (peers, *shard.shape)), axis, 0, 0, tiled=True
    )


def joined_along(pieces, dim):
    pieces = jnp.moveaxis(pieces, 0, dim)
    dims = pieces.shape
    return pieces.reshape(*dims[:dim], dims[dim] * dims[dim + 1], *dims[dim + 2 :])


def gathered_copies(shard, axis, dim):
    pieces = copy_for_each(shard, axis)
    return joined_along(pieces, dim)


def cut_along(shard, dim, peers):
    dims = shard.shape
    pieces = shard.reshape(*dims[:dim], peers, dims[dim] // peers, *dims[dim + 1 :])
    return jnp.moveaxis(pieces, dim, 0)


def sent_and_summed(shard, axis, dim):
    pieces = cut_along(shard, dim, lax.axis_size(axis))
    arrived = lax.all_to_all(pieces, axis, split_axis=0, concat_axis=0, tiled=True)
    return arrived.sum(axis=0)


def frac_turns(values):
    return values - jnp.floor(values)


def hann_window(length):
    frame_steps = jnp.arange(length).astype(jnp.float32)
    return 0.5 - 0.5 * jnp.cos(TWO_PI / length * (frame_steps + 0.5))


def combine(products):
    real_part = products[:, 0, :, 0] - products[:, 1, :, 1]
    imag_part = -(products[:, 1, :, 0] + products[:, 0, :, 1])
    return jnp.stack([real_part, imag_part], axis=1)


def transform(series):
    length = series.shape[0]
    window = hann_window(length)
    energy = jnp.sum(window * window)
    weighted = series * window[:, None, None, None, None]
    frame_steps = jnp.arange(length)
    phase_turns = (frame_steps[:, None] * frame_steps[None, :] % length).astype(jnp.float32)
    dft_angle = TWO_PI / length * phase_turns
    cos_table = jnp.cos(dft_angle)
    sin_table = jnp.sin(dft_angle)
    real_part = weighted[:, :, 0]
    imag_part = weighted[:, :, 1]
    highest = lax.Precision.HIGHEST
    spec_real = jnp.einsum("ft,tsmj->fsmj", cos_table, real_part, precision=highest) + jnp.einsum(
        "ft,tsmj->fsmj", sin_table, imag_part, precision=highest
    )
    spec_imag = jnp.einsum("ft,tsmj->fsmj", cos_table, imag_part, precision=highest) - jnp.einsum(
        "ft,tsmj->fsmj", sin_table, real_part, precision=highest
    )
    oxygen_pair = spec_real[:, 0] * spec_real[:, 0] + spec_imag[:, 0] * spec_imag[:, 0]
    cross_pair = spec_real[:, 0] * spec_real[:, 1] + spec_imag[:, 0] * spec_imag[:, 1]
    hydrogen_pair = spec_real[:, 1] * spec_real[:, 1] + spec_imag[:, 1] * spec_imag[:, 1]
    return jnp.stack([oxygen_pair, cross_pair, hydrogen_pair]) / energy


def power_rows(base_cos, base_sin, count):
    rows = [(jnp.ones_like(base_cos), jnp.zeros_like(base_sin)), (base_cos, base_sin)]
    for _ in range(count - 1):
        prev_cos, prev_sin = rows[-1]
        rows.append((prev_cos * base_cos - prev_sin * base_sin, prev_sin * base_cos + prev_cos * base_sin))
    return rows


def split_dot(picks, table, stacked):
    rows = table.shape[0]
    high = table.astype(jnp.bfloat16)
    stacked[0:rows, :] = high
    stacked[rows : 2 * rows, :] = (table - high.astype(jnp.float32)).astype(jnp.bfloat16)
    dims = (((1,), (0,)), ((), ()))
    return lax.dot_general(picks, stacked[...], dims, preferred_element_type=jnp.float32)


def frame_kernel(base_ref, onehot_ref, pick_x_ref, pick_y_ref, pick_z_ref, out_ref, axis_all, x_all, yz_all, xh_all):
  for f in range(base_ref.shape[0]):
    axis_ref = axis_all.at[f]
    x_ref = x_all.at[f]
    yz_half = yz_all.at[f]
    x_half = xh_all.at[f]
    base = base_ref[f]
    kmax = 16
    rows_pad = axis_ref.shape[1]
    for axis in range(2):
        powers = power_rows(base[2 + 2 * axis : 3 + 2 * axis], base[3 + 2 * axis : 4 + 2 * axis], kmax)
        for k, (cos_k, sin_k) in enumerate(powers):
            axis_ref[2 * axis, kmax + k : kmax + k + 1, :] = cos_k
            axis_ref[2 * axis + 1, kmax + k : kmax + k + 1, :] = sin_k
            if k:
                axis_ref[2 * axis, kmax - k : kmax - k + 1, :] = cos_k
                axis_ref[2 * axis + 1, kmax - k : kmax - k + 1, :] = -sin_k
        pad = rows_pad - (2 * kmax + 1)
        zeros = jnp.zeros((pad, base.shape[1]), jnp.float32)
        axis_ref[2 * axis, 2 * kmax + 1 :, :] = zeros
        axis_ref[2 * axis + 1, 2 * kmax + 1 :, :] = zeros
    x_powers = power_rows(base[0:1], base[1:2], kmax)
    for k in range(1, kmax + 1):
        x_ref[0, k - 1 : k, :] = x_powers[k][0]
        x_ref[1, k - 1 : k, :] = x_powers[k][1]
    pick_x = pick_x_ref[...]
    pick_y = pick_y_ref[...]
    pick_z = pick_z_ref[...]
    cy = split_dot(pick_y, axis_ref[0], yz_half.at[0])
    sy = split_dot(pick_y, axis_ref[1], yz_half.at[1])
    cz = split_dot(pick_z, axis_ref[2], yz_half.at[2])
    sz = split_dot(pick_z, axis_ref[3], yz_half.at[3])
    yz_cos = (cy * cz - sy * sz).astype(jnp.bfloat16)
    yz_sin = (sy * cz + cy * sz).astype(jnp.bfloat16)
    x_cos = split_dot(pick_x, x_ref[0], x_half.at[0])
    x_sin = split_dot(pick_x, x_ref[1], x_half.at[1])
    onehot = onehot_ref[...]
    x_table = jnp.concatenate(
        [onehot[0:1] * x_cos, onehot[0:1] * x_sin, onehot[1:2] * x_cos, onehot[1:2] * x_sin], axis=0
    ).astype(jnp.bfloat16)
    dims = (((1,), (1,)), ((), ()))
    with_cos = lax.dot_general(x_table, yz_cos, dims, preferred_element_type=jnp.float32)
    with_sin = lax.dot_general(x_table, yz_sin, dims, preferred_element_type=jnp.float32)
    kx = kmax
    for s in range(2):
        cos_rows = slice((2 * s) * kx, (2 * s + 1) * kx)
        sin_rows = slice((2 * s + 1) * kx, (2 * s + 2) * kx)
        real_part = with_cos[cos_rows] - with_sin[sin_rows]
        imag_part = -(with_sin[cos_rows] + with_cos[sin_rows])
        share = kx // out_ref.shape[0]
        for peer in range(out_ref.shape[0]):
            out_ref[peer, f, s, 0] = real_part[peer * share : (peer + 1) * share]
            out_ref[peer, f, s, 1] = imag_part[peer * share : (peer + 1) * share]


def picks_of(index, lowest, count):
    cols = jnp.arange(count, dtype=jnp.int32)
    picks = (index[:, None] - lowest == cols[None, :]).astype(jnp.bfloat16)
    return jnp.concatenate([picks, picks], axis=1)


def local(positions, species, kx_index, kyz_index):
    local_frames = positions.shape[0]
    kx_count = kx_index.shape[0]
    kyz_local = kyz_index.shape[1]
    total_atoms = positions.shape[2] * lax.axis_size("atom") * lax.axis_size("wave")
    onehot_all = jnp.stack([species == 0, species == 1]).astype(jnp.float32)
    flat = positions.size
    lane_rows = flat // 128 if flat % 128 == 0 else 1
    packed = copy_for_each(positions.reshape(lane_rows, flat // lane_rows), "wave")
    peers = lax.axis_size("wave")
    block_coords = joined_along(packed.reshape(peers, *positions.shape), 2)
    atom_count = block_coords.shape[2]
    angle = TWO_PI * frac_turns(block_coords)
    base = jnp.stack([jnp.cos(angle), jnp.sin(angle)], axis=2).reshape(local_frames, 6, atom_count)
    rows_pad = 48
    atom_peers = lax.axis_size("atom")
    frames_per_step = math.gcd(local_frames, 8)
    pick_x = picks_of(kx_index, 1, 16)
    pick_y = picks_of(kyz_index[0], -16, rows_pad)
    pick_z = picks_of(kyz_index[1], -16, rows_pad)
    partial_value = pl.pallas_call(
        frame_kernel,
        grid=(local_frames // frames_per_step,),
        in_specs=[
            pl.BlockSpec((frames_per_step, 6, atom_count), lambda t: (t, 0, 0)),
            pl.BlockSpec((2, atom_count), lambda t: (0, 0)),
            pl.BlockSpec((kx_count, 32), lambda t: (0, 0)),
            pl.BlockSpec((kyz_local, 2 * rows_pad), lambda t: (0, 0)),
            pl.BlockSpec((kyz_local, 2 * rows_pad), lambda t: (0, 0)),
        ],
        out_specs=pl.BlockSpec((atom_peers, frames_per_step, 2, 2, kx_count // atom_peers, kyz_local), lambda t: (0, t, 0, 0, 0, 0)),
        out_shape=jax.ShapeDtypeStruct((atom_peers, local_frames, 2, 2, kx_count // atom_peers, kyz_local), jnp.float32),
        scratch_shapes=[
            pltpu.VMEM((frames_per_step, 4, rows_pad, atom_count), jnp.float32),
            pltpu.VMEM((frames_per_step, 2, 16, atom_count), jnp.float32),
            pltpu.VMEM((frames_per_step, 4, 2 * rows_pad, atom_count), jnp.bfloat16),
            pltpu.VMEM((frames_per_step, 2, 32, atom_count), jnp.bfloat16),
        ],
    )(base, onehot_all, pick_x, pick_y, pick_z)
    owned = lax.all_to_all(partial_value, "atom", split_axis=0, concat_axis=0, tiled=True).sum(axis=0)
    densities = owned / jnp.sqrt(jnp.float32(total_atoms))
    spectra = transform(lax.all_to_all(densities, "tm", split_axis=3, concat_axis=0, tiled=True))
    return (spectra, densities)


def solution(mesh):
    in_specs = (P("tm", None, ("atom", "wave")), P("atom"), P(), P(None, "wave"))
    out_specs = (P(None, None, ("atom", "tm"), "wave"), P("tm", None, None, "atom", "wave"))
    return jax.shard_map(local, mesh=mesh, in_specs=in_specs, out_specs=out_specs, check_vma=False)
```
